256 devices in a mesh: dp: 32 (over z, y_hi, core), inner: 8 (over y_lo, x).
Axes of the slice: x: 4, y: 4 (y_hi: 2, y_lo: 2; y = y_hi * 2 + y_lo), z: 8, core: 2. Of those that a mesh axis runs over, the one named last changes fastest.
Arguments:
- tokens: bfloat16 [131072, 1664], P(('dp', 'inner')), may hold values from -16 to 16
- attn_gain: float32 [1664], replicated, may hold values from 0.1 to 1.9
- qkv_weight: bfloat16 [3, 1664, 832], P(None, 'dp', 'inner'), may hold values from -6 to 6
- out_weight: bfloat16 [832, 1664], P('inner', 'dp'), may hold values from -0.21875 to 0.21875
- merge_gain: float32 [6656], replicated, may hold values from 0.25 to 1.75
- merge_weight: bfloat16 [6656, 2048], P('dp', 'inner'), may hold values from -0.078125 to 0.078125
- segment_ids: int32 [131072], P('dp'), may hold values from -1 to 7, as said below
- owners: int32 [32768, 1], P('dp'), may hold values from 0 to 31; in each aligned block of 1024 rows (0 to 1023, 1024 to 2047, ...) at most 64 rows name the same one
Outputs:
- merged_out: bfloat16 [65536, 2048], P('dp', 'inner')
The draws below stay inside these ranges and needn't reach their ends.
Inputs may be any that keep to these rules, and one draw needn't show every extreme that they name: `segment_ids`: within each device's aligned block of 512 tokens, ids never fall except to -1, which fills a tail of 4 or more tokens; every run of one id starts at a multiple of 4 and holds a multiple of 4 tokens. `owners`: in each aligned block of 1024 rows (the rows of one index of dp) no owner is named by more than 64 rows.
All inputs are finite; a program needn't handle non-finite values.
Results may differ from the reference program's by a relative error of at most 0.0062.
Values may be sent and summed in bfloat16 or wider, within the bound.
No kernel may reach another device: no remote copies, remote signals or barrier semaphores. Data moves between devices by JAX's collectives and lax.ppermute only.
A program may use at most 128 MiB of HBM per device.

```python
import math
import jax
import jax.numpy as jnp
import numpy as np
from jax import lax

D = 1664
HEAD_DIM = 104
HEADS = 8
M_OUT = 2048
TOK_DEV = 512
IMG_DEV = 8
HD = 832
MQ_DEV = 128
TOKENS = 131072
MERGED = 32768
GROUP = 1024
SLOT = 64
ROWS_OWNER = 2048
OUT_ROWS = 65536
N_DP = 32
N_INNER = 8


def draw_tokens(key, part):
    key_rows, key_cols, key_noise = jax.random.split(key, 3)
    row_scale = jnp.exp(jax.random.uniform(key_rows, (TOKENS, 1), jnp.float32, math.log(0.1), 0.0))
    col_scale = jnp.exp(jax.random.uniform(key_cols, (1, D), jnp.float32, math.log(0.3), math.log(3.0)))
    noise = jnp.clip(jax.random.normal(key_noise, (TOKENS, D), jnp.float32), -4.0, 4.0)
    values = noise * col_scale * row_scale
    return values.astype(jnp.bfloat16)


def draw_qkv_weight(key, part):
    key_base = jax.random.fold_in(key, 0)
    base = jnp.clip(jax.random.normal(key_base, (3, D, HEADS, HEAD_DIM), jnp.float32), -4.0, 4.0) * D ** (-0.5)
    return base.reshape(3, D, HEADS * HEAD_DIM).astype(jnp.bfloat16)


def draw_segment_ids(key, part):
    blocks = TOKENS // TOK_DEV
    quads = TOK_DEV // 4
    key_ids, key_pad = jax.random.split(key)
    raw = jax.random.randint(key_ids, (blocks, quads), 0, IMG_DEV)
    ids = jnp.sort(raw, axis=1)
    padding = jax.random.randint(key_pad, (blocks, 1), 1, quads // 4 + 1)
    place = jnp.arange(quads)[None, :]
    live = quads - padding
    ids = jnp.where(place == live - 1, IMG_DEV - 1, ids)
    ids = jnp.where(place >= live, -1, ids)
    return jnp.repeat(ids, 4, axis=1).reshape(TOKENS).astype(jnp.int32)


def block_levels(own_key, dims, shards, smallest, high):
    def one(dim, shards_of):
        steps = jax.random.uniform(jax.random.fold_in(jax.random.fold_in(own_key, 6), dim), (shards_of,), jnp.float32, smallest / len(shards), high / len(shards))
        return jnp.repeat(jnp.exp(steps), dims[dim] // shards_of).reshape((-1,) + (1,) * (len(dims) - dim - 1))

    level = one(*shards[0])
    for cut in shards[1:]:
        level = level * one(*cut)
    return level


def assign_block(own_key, own, number, rows, amount, top, bound, lean):
    sequence = jax.random.permutation(own_key, amount)
    packed, usual = load_shares(amount, rows * top, bound, lean, True), load_shares(amount, rows * top, bound, lean, False)
    places = jnp.arange(amount)

    def named(lengths, rotation):
        used = int((lengths > 0).sum())
        fixed = max(1, used // 4)
        passed = fixed + (places - fixed + rotation * (used - fixed)) % max(1, amount - fixed)
        return jnp.zeros((amount,), jnp.int32).at[sequence[jnp.where(places < fixed, places, passed)]].set(jnp.asarray(lengths, jnp.int32))

    lengths = jnp.where(number % 4 == 0, named(packed, number // 4), named(usual, number - number // 4 - 1))
    mixed = jax.random.permutation(jax.random.fold_in(own, 3), amount)
    source_of, sink = mixed[0:amount // 2 * 2:2], mixed[1:amount // 2 * 2:2]
    slack = jnp.minimum(lengths[source_of] - 1, bound - lengths[sink]) // 2
    slack = jnp.where((source_of == sequence[0]) | (sink == sequence[0]) | (lengths[sink] == 0), 0, jnp.maximum(slack, 0))
    passed = jax.random.randint(jax.random.fold_in(own, 4), (amount // 2,), 0, 1 << 20) % (slack + 1)
    lengths = lengths.at[source_of].add(-passed).at[sink].add(passed)
    members = jnp.searchsorted(jnp.cumsum(lengths), jnp.arange(rows * top), side="right").astype(jnp.int32)
    listing = members.reshape(top, rows).T
    listing = listing[jax.random.permutation(jax.random.fold_in(own, 1), rows)]
    rotation = jax.random.randint(jax.random.fold_in(own, 2), (rows, 1), 0, top)
    return jnp.take_along_axis(listing, (jnp.arange(top)[None, :] + rotation) % top, axis=1)


def load_shares(number_of, total, limit, skew, full):
    weights = [(1 << 20) // math.isqrt(rank ** skew) + 1 for rank in range(1, number_of + 1)]
    largest = limit if full else min(limit, max(-(-total // number_of), total * weights[0] // sum(weights)))
    least = 1 if total - largest >= number_of - 1 else 0
    given, rest = [largest] + [least] * (number_of - 1), total - largest - least * (number_of - 1)
    while rest > 0:
        free = [i for i in range(1, number_of) if given[i] < largest] or [i for i in range(1, number_of) if given[i] < limit]
        mass, remaining = sum([weights[i] for i in free]), rest
        for i in free:
            extra = min(limit - given[i], max(1, remaining * weights[i] // mass), rest)
            given[i] = given[i] + extra
            rest = rest - extra
    return np.array(given)


def scatter_about(rng, shape, scale, bound, cuts=(), kind=jnp.bfloat16):
    drawn = scale * jax.random.normal(rng, shape, jnp.float32)
    if cuts:
        drawn = drawn * block_levels(rng, shape, cuts, -0.22, 0.18)
    return jnp.clip(drawn, -bound, bound).astype(kind)


def setup_inputs(seed: int = 0) -> dict:
    splits = jax.random.split(jax.random.key(seed), 9)
    tokens = draw_tokens(jax.random.fold_in(splits[8], 71), 0)
    attn_gain = jnp.clip(1.0 + 0.18 * jax.random.normal(splits[1], (D,), jnp.float32), 0.1, 1.9)
    qkv_weight = draw_qkv_weight(jax.random.fold_in(splits[8], 71), 0)
    out_weight = scatter_about(splits[3], (HD, D), HD ** -0.5, 0.21875, ((0, 8), (1, 32)))
    merge_gain = jnp.clip(1.0 + 0.15 * jax.random.normal(splits[4], (4 * D,), jnp.float32), 0.25, 1.75)
    merge_weight = scatter_about(splits[5], (4 * D, M_OUT), (4 * D) ** -0.5, 0.078125, ((0, 32), (1, 8)))
    segment_ids = draw_segment_ids(jax.random.fold_in(splits[8], 71), 0)
    owners_keys = jax.random.split(jax.random.fold_in(splits[7], 1), MERGED // GROUP)
    owners_turns = jax.random.permutation(jax.random.fold_in(splits[7], 3), MERGED // GROUP)
    owners = jax.vmap(lambda own, number: assign_block(jax.random.fold_in(splits[7], 2), own, number, GROUP, N_DP, 1, SLOT, 2))(owners_keys, owners_turns).reshape((MERGED, 1))
    return dict(tokens=tokens, attn_gain=attn_gain, qkv_weight=qkv_weight, out_weight=out_weight, merge_gain=merge_gain, merge_weight=merge_weight, segment_ids=segment_ids, owners=owners)


EPS = 1e-06
NEG = -1e+30

def layer_norm(values, gain):
    values = values.astype(jnp.float32)
    center = values - lax.optimization_barrier(jnp.mean(values, axis=-1, keepdims=True))
    spread = lax.optimization_barrier(jnp.mean(center * center, axis=-1, keepdims=True))
    return center * lax.rsqrt(spread + EPS) * gain

def attend(queries, keys, vectors, segment):
    scores = jnp.einsum('qhe,khe->hqk', queries.astype(jnp.float32), keys.astype(jnp.float32)) * HEAD_DIM ** (-0.5)
    visible = segment[:, None] == segment[None, :]
    scores = jnp.where(visible[None, :, :], scores, NEG)
    top = lax.optimization_barrier(jnp.max(scores, axis=-1, keepdims=True))
    weights = jnp.exp(scores - top)
    probs = (weights / lax.optimization_barrier(jnp.sum(weights, axis=-1, keepdims=True))).astype(jnp.bfloat16)
    context = jnp.einsum('hqk,khe->qhe', probs.astype(jnp.float32), vectors.astype(jnp.float32))
    return context.astype(jnp.bfloat16)

def reference(tokens, attn_gain, qkv_weight, out_weight, merge_gain, merge_weight, segment_ids, owners):

    def encode_block(inputs):
        block, segment = inputs
        normed = layer_norm(block, attn_gain).astype(jnp.bfloat16)
        projected = jnp.einsum('td,cdh->cth', normed.astype(jnp.float32), qkv_weight.astype(jnp.float32))
        projected = projected.astype(jnp.bfloat16).reshape(3, TOK_DEV, HEADS, HEAD_DIM)
        context = attend(projected[0], projected[1], projected[2], segment).reshape(TOK_DEV, HD)
        hidden = block.astype(jnp.float32) + jnp.dot(context, out_weight, preferred_element_type=jnp.float32)
        quad_rows = hidden.reshape(MQ_DEV, 4 * D)
        live = segment.reshape(MQ_DEV, 4)[:, 0] >= 0
        merged = jnp.where(live[:, None], layer_norm(quad_rows, merge_gain), 0.0).astype(jnp.bfloat16)
        return jnp.dot(merged, merge_weight, preferred_element_type=jnp.float32).astype(jnp.bfloat16)
    blocks = tokens.reshape(N_DP * N_INNER, TOK_DEV, D)
    segments = segment_ids.reshape(N_DP * N_INNER, TOK_DEV)
    features = lax.map(encode_block, (blocks, segments)).reshape(MERGED, M_OUT)
    owner_col = owners[:, 0].astype(jnp.int32)
    chosen = (owner_col[:, None] == jnp.arange(N_DP, dtype=jnp.int32)[None, :]).astype(jnp.int32)
    chosen = chosen.reshape(N_DP, GROUP, N_DP)
    earlier = jnp.cumsum(chosen, axis=1) - chosen
    rank = lax.optimization_barrier(jnp.sum(earlier * chosen, axis=2)).reshape(MERGED).astype(jnp.int32)
    source = (jnp.arange(MERGED, dtype=jnp.int32) // GROUP).astype(jnp.int32)
    target = owner_col * ROWS_OWNER + source * SLOT + rank
    return jnp.zeros((OUT_ROWS, M_OUT), jnp.bfloat16).at[target].set(features)
```

```python
import jax
import jax.numpy as jnp
from jax import lax
from jax.sharding import PartitionSpec as P

HEAD_DIM = 104


EPS = 1e-06
NEG = -1e30


def layer_norm(values, gain):
    values = values.astype(jnp.float32)
    center = values - jnp.mean(values, axis=-1, keepdims=True)
    spread = jnp.mean(center * center, axis=-1, keepdims=True)
    return center * lax.rsqrt(spread + EPS) * gain


def attend_block(queries, keys, vectors, segment):
    scale = queries.shape[-1] ** (-0.5)
    scores = jnp.einsum("qhe,khe->hqk", queries, keys, preferred_element_type=jnp.float32) * scale
    visible = segment[:, None] == segment[None, :]
    scores = jnp.where(visible[None, :, :], scores, NEG)
    top = jnp.max(scores, axis=-1, keepdims=True)
    weights = jnp.exp(scores - top)
    probs = (weights / jnp.sum(weights, axis=-1, keepdims=True)).astype(jnp.bfloat16)
    context = jnp.einsum("hqk,khe->qhe", probs, vectors, preferred_element_type=jnp.float32)
    return context.astype(jnp.bfloat16)


def split_heads(projected):
    shaped = projected.reshape(3, projected.shape[1], projected.shape[2] // HEAD_DIM, HEAD_DIM)
    return (shaped[0], shaped[1], shaped[2])


def gather_weights(qkv_weight, out_weight, merge_weight):
    n_dp = lax.axis_size("dp")
    n_in = lax.axis_size("inner")
    qkv_n = qkv_weight.size
    out_n = out_weight.size
    first = jnp.concatenate([qkv_weight.reshape(-1), out_weight.reshape(-1)])
    first = lax.all_gather(first, "inner", axis=0, tiled=False)
    second = jnp.concatenate([first.reshape(-1), merge_weight.reshape(-1)])
    second = lax.all_gather(second, "dp", axis=0, tiled=False)
    pair = second[:, : n_in * (qkv_n + out_n)].reshape(n_dp, n_in, qkv_n + out_n)
    qkv_full = pair[:, :, :qkv_n].reshape((n_dp, n_in) + qkv_weight.shape)
    out_full = pair[:, :, qkv_n:].reshape((n_dp, n_in) + out_weight.shape)
    merge_full = second[:, n_in * (qkv_n + out_n) :].reshape(
        (n_dp * merge_weight.shape[0], merge_weight.shape[1])
    )
    return qkv_full, out_full, merge_full


def local(tokens, attn_gain, qkv_weight, out_weight, merge_gain, merge_weight, segment_ids, owners):
    tok_rows = tokens.shape[0]
    n_dp = lax.axis_size("dp")
    local_segment = lax.dynamic_slice_in_dim(
        segment_ids, lax.axis_index("inner") * tok_rows, tok_rows
    )
    qkv_full, out_full, merge_full = gather_weights(qkv_weight, out_weight, merge_weight)
    normed = layer_norm(tokens, attn_gain).astype(jnp.bfloat16)
    projected = jnp.einsum(
        "tgk,gjcke->ctje",
        normed.reshape(tok_rows, n_dp, -1),
        qkv_full,
        preferred_element_type=jnp.float32,
    ).astype(jnp.bfloat16)
    queries, keys, vectors = projected[0], projected[1], projected[2]
    context = attend_block(queries, keys, vectors, local_segment)
    attn_out = jnp.einsum(
        "tje,gjek->tgk", context, out_full, preferred_element_type=jnp.float32
    ).reshape(tok_rows, -1)
    hidden = tokens.astype(jnp.float32) + attn_out
    quad_rows = hidden.reshape(tok_rows // 4, -1)
    live = local_segment.reshape(-1, 4)[:, 0] >= 0
    merged = jnp.where(live[:, None], layer_norm(quad_rows, merge_gain), 0.0).astype(jnp.bfloat16)
    features = jnp.dot(
        lax.all_gather(merged, "inner", axis=0, tiled=True),
        merge_full,
        preferred_element_type=jnp.float32,
    ).astype(jnp.bfloat16)
    group_rows = features.shape[0]
    slots = 2 * group_rows // n_dp
    owner_col = owners[:, 0]
    chosen = (owner_col[:, None] == jnp.arange(n_dp, dtype=jnp.int32)[None, :]).astype(jnp.int32)
    earlier = jnp.cumsum(chosen, axis=0) - chosen
    rank = jnp.sum(earlier * chosen, axis=1)
    target = owner_col * slots + rank
    source_row = (
        jnp.full((n_dp * slots,), group_rows, jnp.int32)
        .at[target]
        .set(jnp.arange(group_rows, dtype=jnp.int32))
    )
    padded = jnp.concatenate([features, jnp.zeros((1, features.shape[1]), jnp.bfloat16)], axis=0)
    outgoing = padded[source_row]
    return lax.all_to_all(outgoing, "dp", split_axis=0, concat_axis=0, tiled=True)


def solution(mesh):
    placed = (
        P(("dp", "inner"), None),
        P(),
        P(None, "dp", "inner"),
        P("inner", "dp"),
        P(),
        P("dp", "inner"),
        P("dp"),
        P("dp", None),
    )
    return jax.shard_map(
        local, mesh=mesh, in_specs=placed, out_specs=P("dp", "inner"), check_vma=False
    )
```

```python
import jax
import jax.numpy as jnp
from jax import lax
from jax.sharding import PartitionSpec as P

HEAD_DIM = 104


EPS = 1e-06
NEG = -1e30


def layer_norm(values, gain):
    values = values.astype(jnp.float32)
    center = values - jnp.mean(values, axis=-1, keepdims=True)
    spread = jnp.mean(center * center, axis=-1, keepdims=True)
    return center * lax.rsqrt(spread + EPS) * gain


def attend_block(queries, keys, vectors, segment):
    scale = queries.shape[-1] ** (-0.5)
    scores = jnp.einsum("qhe,khe->hqk", queries, keys, preferred_element_type=jnp.float32) * scale
    visible = segment[:, None] == segment[None, :]
    scores = jnp.where(visible[None, :, :], scores, NEG)
    top = jnp.max(scores, axis=-1, keepdims=True)
    weights = jnp.exp(scores - top)
    probs = (weights / jnp.sum(weights, axis=-1, keepdims=True)).astype(jnp.bfloat16)
    context = jnp.einsum("hqk,khe->qhe", probs, vectors, preferred_element_type=jnp.float32)
    return context.astype(jnp.bfloat16)


def split_heads(projected):
    shaped = projected.reshape(3, projected.shape[1], projected.shape[2] // HEAD_DIM, HEAD_DIM)
    return (shaped[0], shaped[1], shaped[2])


def round8(rows):
    return -(-rows // 8) * 8


def pad_rows(block):
    return jnp.pad(block, ((0, round8(block.shape[0]) - block.shape[0]), (0, 0)))


def gather_weights(qkv_weight, out_weight):
    slabs = [pad_rows(qkv_weight[c]) for c in range(3)] + [pad_rows(out_weight.T)]
    stacked = jnp.concatenate(slabs, axis=0)
    stacked = lax.all_gather(stacked, "inner", axis=1, tiled=True)
    stacked = lax.all_gather(stacked, "dp", axis=0, tiled=False)
    return stacked.reshape(stacked.shape[0], 4, -1, stacked.shape[-1])


def local(tokens, attn_gain, qkv_weight, out_weight, merge_gain, merge_weight, segment_ids, owners):
    tok_rows = tokens.shape[0]
    n_dp = lax.axis_size("dp")
    local_segment = lax.dynamic_slice_in_dim(
        segment_ids, lax.axis_index("inner") * tok_rows, tok_rows
    )
    gathered = gather_weights(qkv_weight, out_weight)
    normed = layer_norm(tokens, attn_gain).astype(jnp.bfloat16)
    normed = normed.reshape(tok_rows, n_dp, -1)
    normed = jnp.pad(normed, ((0, 0), (0, 0), (0, round8(normed.shape[-1]) - normed.shape[-1])))
    projected = jnp.einsum(
        "tgk,gckh->cth",
        normed,
        gathered[:, :3],
        preferred_element_type=jnp.float32,
    ).astype(jnp.bfloat16)
    queries, keys, vectors = split_heads(projected)
    context = attend_block(queries, keys, vectors, local_segment).reshape(tok_rows, -1)
    attn_out = jnp.einsum(
        "tf,gkf->tgk", context, gathered[:, 3], preferred_element_type=jnp.float32
    )
    attn_out = attn_out[:, :, : tokens.shape[1] // n_dp].reshape(tok_rows, -1)
    hidden = tokens.astype(jnp.float32) + attn_out
    quad_rows = hidden.reshape(tok_rows // 4, -1)
    live = local_segment.reshape(-1, 4)[:, 0] >= 0
    merged = jnp.where(live[:, None], layer_norm(quad_rows, merge_gain), 0.0).astype(jnp.bfloat16)
    features = jnp.dot(
        lax.all_gather(merged, "inner", axis=0, tiled=True),
        lax.all_gather(merge_weight, "dp", axis=0, tiled=True),
        preferred_element_type=jnp.float32,
    ).astype(jnp.bfloat16)
    group_rows = features.shape[0]
    slots = 2 * group_rows // n_dp
    owner_col = owners[:, 0]
    chosen = (owner_col[:, None] == jnp.arange(n_dp, dtype=jnp.int32)[None, :]).astype(jnp.int32)
    earlier = jnp.cumsum(chosen, axis=0) - chosen
    rank = jnp.sum(earlier * chosen, axis=1)
    target = owner_col * slots + rank
    source_row = (
        jnp.full((n_dp * slots,), group_rows, jnp.int32)
        .at[target]
        .set(jnp.arange(group_rows, dtype=jnp.int32))
    )
    padded = jnp.concatenate([features, jnp.zeros((1, features.shape[1]), jnp.bfloat16)], axis=0)
    outgoing = padded[source_row]
    return lax.all_to_all(outgoing, "dp", split_axis=0, concat_axis=0, tiled=True)


def solution(mesh):
    placed = (
        P(("dp", "inner"), None),
        P(),
        P(None, "dp", "inner"),
        P("inner", "dp"),
        P(),
        P("dp", "inner"),
        P("dp"),
        P("dp", None),
    )
    return jax.shard_map(
        local, mesh=mesh, in_specs=placed, out_specs=P("dp", "inner"), check_vma=False
    )
```

```python
import jax
import jax.numpy as jnp
from jax import lax
from jax.sharding import Mesh, PartitionSpec as P

HEAD_DIM = 104


EPS = 1e-06
NEG = -1e30


def layer_norm(values, gain):
    values = values.astype(jnp.float32)
    center = values - jnp.mean(values, axis=-1, keepdims=True)
    spread = jnp.mean(center * center, axis=-1, keepdims=True)
    return center * lax.rsqrt(spread + EPS) * gain


def attend_block(queries, keys, vectors, segment):
    scale = queries.shape[-1] ** (-0.5)
    scores = jnp.einsum("qhe,khe->hqk", queries, keys, preferred_element_type=jnp.float32) * scale
    visible = segment[:, None] == segment[None, :]
    scores = jnp.where(visible[None, :, :], scores, NEG)
    top = jnp.max(scores, axis=-1, keepdims=True)
    weights = jnp.exp(scores - top)
    probs = (weights / jnp.sum(weights, axis=-1, keepdims=True)).astype(jnp.bfloat16)
    context = jnp.einsum("hqk,khe->qhe", probs, vectors, preferred_element_type=jnp.float32)
    return context.astype(jnp.bfloat16)


def split_heads(projected):
    shaped = projected.reshape(3, projected.shape[1], projected.shape[2] // HEAD_DIM, HEAD_DIM)
    return (shaped[0], shaped[1], shaped[2])


def round8(rows):
    return -(-rows // 8) * 8


def pad_rows(block):
    return jnp.pad(block, ((0, round8(block.shape[0]) - block.shape[0]), (0, 0)))


def gather_dp(block):
    halves = lax.all_gather(block, "dq", axis=0, tiled=False)
    whole = lax.all_gather(halves, "core", axis=1, tiled=False)
    return whole.reshape((-1,) + block.shape)


def gather_weights(qkv_weight, out_weight):
    slabs = [pad_rows(qkv_weight[c]) for c in range(3)] + [pad_rows(out_weight.T)]
    stacked = jnp.concatenate(slabs, axis=0)
    stacked = lax.all_gather(stacked, "inner", axis=1, tiled=True)
    stacked = gather_dp(stacked)
    return stacked.reshape(stacked.shape[0], 4, -1, stacked.shape[-1])


def local(tokens, attn_gain, qkv_weight, out_weight, merge_gain, merge_weight, segment_ids, owners):
    tok_rows = tokens.shape[0]
    n_dp = lax.axis_size("dq") * lax.axis_size("core")
    local_segment = lax.dynamic_slice_in_dim(
        segment_ids, lax.axis_index("inner") * tok_rows, tok_rows
    )
    gathered = gather_weights(qkv_weight, out_weight)
    merge_weight, gathered = lax.optimization_barrier((merge_weight, gathered))
    normed = layer_norm(tokens, attn_gain).astype(jnp.bfloat16)
    normed = normed.reshape(tok_rows, n_dp, -1)
    normed = jnp.pad(normed, ((0, 0), (0, 0), (0, round8(normed.shape[-1]) - normed.shape[-1])))
    projected = jnp.einsum(
        "tgk,gckh->cth",
        normed,
        gathered[:, :3],
        preferred_element_type=jnp.float32,
    ).astype(jnp.bfloat16)
    queries, keys, vectors = split_heads(projected)
    context = attend_block(queries, keys, vectors, local_segment).reshape(tok_rows, -1)
    attn_out = jnp.einsum(
        "tf,gkf->tgk", context, gathered[:, 3], preferred_element_type=jnp.float32
    )
    attn_out = attn_out[:, :, : tokens.shape[1] // n_dp].reshape(tok_rows, -1)
    hidden = tokens.astype(jnp.float32) + attn_out
    quad_rows = hidden.reshape(tok_rows // 4, -1)
    live = local_segment.reshape(-1, 4)[:, 0] >= 0
    merged = jnp.where(live[:, None], layer_norm(quad_rows, merge_gain), 0.0).astype(jnp.bfloat16)
    features = jnp.dot(
        lax.all_gather(merged, "inner", axis=0, tiled=True),
        gather_dp(merge_weight).reshape(-1, merge_weight.shape[1]),
        preferred_element_type=jnp.float32,
    ).astype(jnp.bfloat16)
    group_rows = features.shape[0]
    slots = 2 * group_rows // n_dp
    owner_col = owners[:, 0]
    chosen = (owner_col[:, None] == jnp.arange(n_dp, dtype=jnp.int32)[None, :]).astype(jnp.int32)
    earlier = jnp.cumsum(chosen, axis=0) - chosen
    rank = jnp.sum(earlier * chosen, axis=1)
    target = owner_col * slots + rank
    source_row = (
        jnp.full((n_dp * slots,), group_rows, jnp.int32)
        .at[target]
        .set(jnp.arange(group_rows, dtype=jnp.int32))
    )
    padded = jnp.concatenate([features, jnp.zeros((1, features.shape[1]), jnp.bfloat16)], axis=0)
    outgoing = padded[source_row]
    return lax.all_to_all(outgoing, ("dq", "core"), split_axis=0, concat_axis=0, tiled=True)


def solution(mesh):
    dp = ("dq", "core")
    n_dp, n_in = mesh.shape["dp"], mesh.shape["inner"]
    split = Mesh(mesh.devices.reshape(n_dp // 2, 2, n_in), ("dq", "core", "inner"))
    placed = (
        P((*dp, "inner"), None),
        P(),
        P(None, dp, "inner"),
        P("inner", dp),
        P(),
        P(dp, "inner"),
        P(dp),
        P(dp, None),
    )
    return jax.shard_map(
        local, mesh=split, in_specs=placed, out_specs=P(dp, "inner"), check_vma=False
    )
```

```python
import jax
import jax.numpy as jnp
from jax import lax
from jax.sharding import PartitionSpec as P

HEAD_DIM = 104


EPS = 1e-06
NEG = -1e30


def layer_norm(values, gain):
    values = values.astype(jnp.float32)
    center = values - jnp.mean(values, axis=-1, keepdims=True)
    spread = jnp.mean(center * center, axis=-1, keepdims=True)
    return center * lax.rsqrt(spread + EPS) * gain


def attend_block(queries, keys, vectors, segment):
    scale = queries.shape[-1] ** (-0.5)
    scores = jnp.einsum("qhe,khe->hqk", queries, keys, preferred_element_type=jnp.float32) * scale
    visible = segment[:, None] == segment[None, :]
    scores = jnp.where(visible[None, :, :], scores, NEG)
    top = jnp.max(scores, axis=-1, keepdims=True)
    weights = jnp.exp(scores - top)
    probs = (weights / jnp.sum(weights, axis=-1, keepdims=True)).astype(jnp.bfloat16)
    context = jnp.einsum("hqk,khe->qhe", probs, vectors, preferred_element_type=jnp.float32)
    return context.astype(jnp.bfloat16)


def split_heads(projected):
    shaped = projected.reshape(3, projected.shape[1], projected.shape[2] // HEAD_DIM, HEAD_DIM)
    return (shaped[0], shaped[1], shaped[2])


def round8(rows):
    return -(-rows // 8) * 8


def pad_rows(block):
    return jnp.pad(block, ((0, round8(block.shape[0]) - block.shape[0]), (0, 0)))


def gather_a2a(block, axis):
    count = lax.axis_size(axis)
    copies = jnp.broadcast_to(block[None], (count,) + block.shape)
    return lax.all_to_all(copies, axis, split_axis=0, concat_axis=0, tiled=True)


def gather_weights(qkv_weight, out_weight):
    slabs = [pad_rows(qkv_weight[c]) for c in range(3)] + [pad_rows(out_weight.T)]
    stacked = jnp.concatenate(slabs, axis=0)
    stacked = lax.all_gather(stacked, "inner", axis=1, tiled=True)
    stacked = gather_a2a(stacked, "dp")
    return stacked.reshape(stacked.shape[0], 4, -1, stacked.shape[-1])


def local(tokens, attn_gain, qkv_weight, out_weight, merge_gain, merge_weight, segment_ids, owners):
    tok_rows = tokens.shape[0]
    n_dp = lax.axis_size("dp")
    local_segment = lax.dynamic_slice_in_dim(
        segment_ids, lax.axis_index("inner") * tok_rows, tok_rows
    )
    gathered = gather_weights(qkv_weight, out_weight)
    normed = layer_norm(tokens, attn_gain).astype(jnp.bfloat16)
    normed = normed.reshape(tok_rows, n_dp, -1)
    normed = jnp.pad(normed, ((0, 0), (0, 0), (0, round8(normed.shape[-1]) - normed.shape[-1])))
    projected = jnp.einsum(
        "tgk,gckh->cth",
        normed,
        gathered[:, :3],
        preferred_element_type=jnp.float32,
    ).astype(jnp.bfloat16)
    queries, keys, vectors = split_heads(projected)
    context = attend_block(queries, keys, vectors, local_segment).reshape(tok_rows, -1)
    attn_out = jnp.einsum(
        "tf,gkf->tgk", context, gathered[:, 3], preferred_element_type=jnp.float32
    )
    attn_out = attn_out[:, :, : tokens.shape[1] // n_dp].reshape(tok_rows, -1)
    hidden = tokens.astype(jnp.float32) + attn_out
    quad_rows = hidden.reshape(tok_rows // 4, -1)
    live = local_segment.reshape(-1, 4)[:, 0] >= 0
    merged = jnp.where(live[:, None], layer_norm(quad_rows, merge_gain), 0.0).astype(jnp.bfloat16)
    features = jnp.dot(
        gather_a2a(merged, "inner").reshape(-1, merged.shape[1]),
        lax.all_gather(merge_weight, "dp", axis=0, tiled=True),
        preferred_element_type=jnp.float32,
    ).astype(jnp.bfloat16)
    group_rows = features.shape[0]
    slots = 2 * group_rows // n_dp
    owner_col = owners[:, 0]
    chosen = (owner_col[:, None] == jnp.arange(n_dp, dtype=jnp.int32)[None, :]).astype(jnp.int32)
    earlier = jnp.cumsum(chosen, axis=0) - chosen
    rank = jnp.sum(earlier * chosen, axis=1)
    target = owner_col * slots + rank
    source_row = (
        jnp.full((n_dp * slots,), group_rows, jnp.int32)
        .at[target]
        .set(jnp.arange(group_rows, dtype=jnp.int32))
    )
    padded = jnp.concatenate([features, jnp.zeros((1, features.shape[1]), jnp.bfloat16)], axis=0)
    outgoing = padded[source_row]
    return lax.all_to_all(outgoing, "dp", split_axis=0, concat_axis=0, tiled=True)


def solution(mesh):
    placed = (
        P(("dp", "inner"), None),
        P(),
        P(None, "dp", "inner"),
        P("inner", "dp"),
        P(),
        P("dp", "inner"),
        P("dp"),
        P("dp", None),
    )
    return jax.shard_map(
        local, mesh=mesh, in_specs=placed, out_specs=P("dp", "inner"), check_vma=False
    )
```

```python
import jax
import jax.numpy as jnp
from jax import lax
from jax.sharding import PartitionSpec as P

HEAD_DIM = 104


EPS = 1e-06
NEG = -1e30


def layer_norm(values, gain):
    values = values.astype(jnp.float32)
    center = values - jnp.mean(values, axis=-1, keepdims=True)
    spread = jnp.mean(center * center, axis=-1, keepdims=True)
    return center * lax.rsqrt(spread + EPS) * gain


def attend_block(queries, keys, vectors, segment):
    scale = queries.shape[-1] ** (-0.5)
    scores = jnp.einsum("qhe,khe->hqk", queries, keys, preferred_element_type=jnp.float32) * scale
    visible = segment[:, None] == segment[None, :]
    scores = jnp.where(visible[None, :, :], scores, NEG)
    top = jnp.max(scores, axis=-1, keepdims=True)
    weights = jnp.exp(scores - top)
    probs = (weights / jnp.sum(weights, axis=-1, keepdims=True)).astype(jnp.bfloat16)
    context = jnp.einsum("hqk,khe->qhe", probs, vectors, preferred_element_type=jnp.float32)
    return context.astype(jnp.bfloat16)


def split_heads(projected):
    shaped = projected.reshape(3, projected.shape[1], projected.shape[2] // HEAD_DIM, HEAD_DIM)
    return (shaped[0], shaped[1], shaped[2])


def round8(rows):
    return -(-rows // 8) * 8


def pad_rows(block):
    return jnp.pad(block, ((0, round8(block.shape[0]) - block.shape[0]), (0, 0)))


def owner_rows(owners, n_dp, group_rows):
    slots = 2 * group_rows // n_dp
    owner_col = owners[:, 0]
    chosen = (owner_col[:, None] == jnp.arange(n_dp, dtype=jnp.int32)[None, :]).astype(jnp.int32)
    earlier = jnp.cumsum(chosen, axis=0) - chosen
    rank = jnp.sum(earlier * chosen, axis=1)
    target = owner_col * slots + rank
    return (
        jnp.full((n_dp * slots,), group_rows, jnp.int32)
        .at[target]
        .set(jnp.arange(group_rows, dtype=jnp.int32))
    )


def local(tokens, attn_gain, qkv_weight, out_weight, merge_gain, merge_weight, segment_ids, owners):
    tok_rows = tokens.shape[0]
    n_dp = lax.axis_size("dp")
    n_in = lax.axis_size("inner")
    lanes = n_in * qkv_weight.shape[-1]
    local_segment = lax.dynamic_slice_in_dim(
        segment_ids, lax.axis_index("inner") * tok_rows, tok_rows
    )
    slabs = [pad_rows(qkv_weight[c]) for c in range(3)] + [pad_rows(out_weight.T)]
    stacked = lax.all_gather(jnp.concatenate(slabs, axis=0), "inner", axis=1, tiled=True)
    merge_rows = -(-merge_weight.size // lanes)
    flat = jnp.pad(merge_weight.reshape(-1), (0, merge_rows * lanes - merge_weight.size))
    payload = jnp.concatenate([stacked, flat.reshape(merge_rows, lanes)], axis=0)
    gathered = lax.all_gather(payload, "dp", axis=0, tiled=False)
    owners, payload = lax.optimization_barrier((owners, payload))
    source_row = owner_rows(owners, n_dp, n_in * tok_rows // 4)
    source_row, tokens = lax.optimization_barrier((source_row, tokens))
    weights = gathered[:, : stacked.shape[0]].reshape(n_dp, 4, -1, lanes)
    merge_full = gathered[:, stacked.shape[0] :].reshape(n_dp, -1)[:, : merge_weight.size]
    merge_full = merge_full.reshape(-1, merge_weight.shape[1])
    normed = layer_norm(tokens, attn_gain).astype(jnp.bfloat16)
    normed = normed.reshape(tok_rows, n_dp, -1)
    normed = jnp.pad(normed, ((0, 0), (0, 0), (0, round8(normed.shape[-1]) - normed.shape[-1])))
    projected = jnp.einsum(
        "tgk,gckh->cth",
        normed,
        weights[:, :3],
        preferred_element_type=jnp.float32,
    ).astype(jnp.bfloat16)
    queries, keys, vectors = split_heads(projected)
    context = attend_block(queries, keys, vectors, local_segment).reshape(tok_rows, -1)
    attn_out = jnp.einsum(
        "tf,gkf->tgk", context, weights[:, 3], preferred_element_type=jnp.float32
    )
    attn_out = attn_out[:, :, : tokens.shape[1] // n_dp].reshape(tok_rows, -1)
    hidden = tokens.astype(jnp.float32) + attn_out
    quad_rows = hidden.reshape(tok_rows // 4, -1)
    live = local_segment.reshape(-1, 4)[:, 0] >= 0
    merged = jnp.where(live[:, None], layer_norm(quad_rows, merge_gain), 0.0).astype(jnp.bfloat16)
    features = jnp.dot(
        lax.all_gather(merged, "inner", axis=0, tiled=True),
        merge_full,
        preferred_element_type=jnp.float32,
    ).astype(jnp.bfloat16)
    group_rows = features.shape[0]
    pick = (source_row[:, None] == jnp.arange(group_rows, dtype=jnp.int32)[None, :]).astype(jnp.bfloat16)
    outgoing = jnp.dot(pick, features, preferred_element_type=jnp.float32).astype(jnp.bfloat16)
    return lax.all_to_all(outgoing, "dp", split_axis=0, concat_axis=0, tiled=True)


def solution(mesh):
    placed = (
        P(("dp", "inner"), None),
        P(),
        P(None, "dp", "inner"),
        P("inner", "dp"),
        P(),
        P("dp", "inner"),
        P("dp"),
        P("dp", None),
    )
    return jax.shard_map(
        local, mesh=mesh, in_specs=placed, out_specs=P("dp", "inner"), check_vma=False
    )
```

```python
import jax
import jax.numpy as jnp
from jax import lax
from jax.sharding import PartitionSpec as P

HEAD_DIM = 104


EPS = 1e-06
NEG = -1e30


def layer_norm(values, gain):
    values = values.astype(jnp.float32)
    center = values - jnp.mean(values, axis=-1, keepdims=True)
    spread = jnp.mean(center * center, axis=-1, keepdims=True)
    return center * lax.rsqrt(spread + EPS) * gain


def attend_block(queries, keys, vectors, segment):
    scale = queries.shape[-1] ** (-0.5)
    scores = jnp.einsum("qhe,khe->hqk", queries, keys, preferred_element_type=jnp.float32) * scale
    visible = segment[:, None] == segment[None, :]
    scores = jnp.where(visible[None, :, :], scores, NEG)
    top = jnp.max(scores, axis=-1, keepdims=True)
    weights = jnp.exp(scores - top)
    probs = (weights / jnp.sum(weights, axis=-1, keepdims=True)).astype(jnp.bfloat16)
    context = jnp.einsum("hqk,khe->qhe", probs, vectors, preferred_element_type=jnp.float32)
    return context.astype(jnp.bfloat16)


def split_heads(projected):
    shaped = projected.reshape(3, projected.shape[1], projected.shape[2] // HEAD_DIM, HEAD_DIM)
    return (shaped[0], shaped[1], shaped[2])


def round8(rows):
    return -(-rows // 8) * 8


def pad_rows(block):
    return jnp.pad(block, ((0, round8(block.shape[0]) - block.shape[0]), (0, 0)))


def owner_rows(owners, n_dp, group_rows):
    slots = 2 * group_rows // n_dp
    owner_col = owners[:, 0]
    chosen = (owner_col[:, None] == jnp.arange(n_dp, dtype=jnp.int32)[None, :]).astype(jnp.int32)
    earlier = jnp.cumsum(chosen, axis=0) - chosen
    rank = jnp.sum(earlier * chosen, axis=1)
    target = owner_col * slots + rank
    return (
        jnp.full((n_dp * slots,), group_rows, jnp.int32)
        .at[target]
        .set(jnp.arange(group_rows, dtype=jnp.int32))
    )


def local(tokens, attn_gain, qkv_weight, out_weight, merge_gain, merge_weight, segment_ids, owners):
    tok_rows = tokens.shape[0]
    n_dp = lax.axis_size("dp")
    n_in = lax.axis_size("inner")
    lanes = n_in * qkv_weight.shape[-1]
    local_segment = lax.dynamic_slice_in_dim(
        segment_ids, lax.axis_index("inner") * tok_rows, tok_rows
    )
    slabs = [pad_rows(qkv_weight[c]) for c in range(3)] + [pad_rows(out_weight.T)]
    stacked = lax.all_gather(jnp.concatenate(slabs, axis=0), "inner", axis=1, tiled=True)
    real = qkv_weight.shape[1]
    tall = round8(real)
    stacked = stacked.reshape(4, tall, lanes)
    merge_rows = -(-merge_weight.size // lanes)
    flat = jnp.pad(merge_weight.reshape(-1), (0, merge_rows * lanes - merge_weight.size))
    flat = flat.reshape(merge_rows, lanes)
    spare = min(4 * (tall - real), merge_rows)
    if spare:
        tail = flat[:spare].reshape(4, spare // 4, lanes)
        tail = jnp.pad(tail, ((0, 0), (0, tall - real - spare // 4), (0, 0)))
        stacked = jnp.concatenate([stacked[:, :real], tail], axis=1)
    rest = flat[spare:]
    extra = -(-rest.shape[0] // tall)
    rest = jnp.pad(rest, ((0, extra * tall - rest.shape[0]), (0, 0))).reshape(extra, tall, lanes)
    payload = jnp.concatenate([stacked, rest], axis=0)
    gathered = lax.all_gather(payload, "dp", axis=0, tiled=False)
    owners, payload = lax.optimization_barrier((owners, payload))
    source_row = owner_rows(owners, n_dp, n_in * tok_rows // 4)
    source_row, tokens = lax.optimization_barrier((source_row, tokens))
    weights = gathered[:, :4]
    merge_full = jnp.concatenate(
        [gathered[:, :4, real:].reshape(n_dp, -1, lanes)[:, :spare], gathered[:, 4:].reshape(n_dp, -1, lanes)],
        axis=1,
    )
    merge_full = merge_full.reshape(n_dp, -1)[:, : merge_weight.size].reshape(-1, merge_weight.shape[1])
    normed = layer_norm(tokens, attn_gain).astype(jnp.bfloat16)
    normed = normed.reshape(tok_rows, n_dp, -1)
    normed = jnp.pad(normed, ((0, 0), (0, 0), (0, round8(normed.shape[-1]) - normed.shape[-1])))
    projected = jnp.einsum(
        "tgk,gckh->cth",
        normed,
        weights[:, :3],
        preferred_element_type=jnp.float32,
    ).astype(jnp.bfloat16)
    queries, keys, vectors = split_heads(projected)
    context = attend_block(queries, keys, vectors, local_segment).reshape(tok_rows, -1)
    attn_out = jnp.einsum(
        "tf,gkf->tgk", context, weights[:, 3], preferred_element_type=jnp.float32
    )
    attn_out = attn_out[:, :, : tokens.shape[1] // n_dp].reshape(tok_rows, -1)
    hidden = tokens.astype(jnp.float32) + attn_out
    width = 4 * hidden.shape[1]
    quad_sum = jnp.sum(hidden, axis=-1).reshape(-1, 4).sum(axis=-1)
    center = hidden - jnp.repeat(quad_sum / width, 4)[:, None]
    quad_sq = jnp.sum(center * center, axis=-1).reshape(-1, 4).sum(axis=-1)
    scale = jnp.repeat(lax.rsqrt(quad_sq / width + EPS), 4)
    gain = jnp.tile(merge_gain.reshape(4, -1), (tok_rows // 4, 1))
    live = jnp.repeat(local_segment.reshape(-1, 4)[:, 0] >= 0, 4)
    merged = jnp.where(live[:, None], center * scale[:, None] * gain, 0.0).astype(jnp.bfloat16)
    merged = merged.reshape(tok_rows // 4, -1)
    features = jnp.dot(
        lax.all_gather(merged, "inner", axis=0, tiled=True),
        merge_full,
        preferred_element_type=jnp.float32,
    ).astype(jnp.bfloat16)
    group_rows = features.shape[0]
    pick = (source_row[:, None] == jnp.arange(group_rows, dtype=jnp.int32)[None, :]).astype(jnp.bfloat16)
    outgoing = jnp.dot(pick, features, preferred_element_type=jnp.float32).astype(jnp.bfloat16)
    return lax.all_to_all(outgoing, "dp", split_axis=0, concat_axis=0, tiled=True)


def solution(mesh):
    placed = (
        P(("dp", "inner"), None),
        P(),
        P(None, "dp", "inner"),
        P("inner", "dp"),
        P(),
        P("dp", "inner"),
        P("dp"),
        P("dp", None),
    )
    return jax.shard_map(
        local, mesh=mesh, in_specs=placed, out_specs=P("dp", "inner"), check_vma=False
    )
```

```python
import jax
import jax.numpy as jnp
from jax import lax
from jax.sharding import Mesh, PartitionSpec as P

HEAD_DIM = 104


EPS = 1e-06
NEG = -1e30


def layer_norm(values, gain):
    values = values.astype(jnp.float32)
    center = values - jnp.mean(values, axis=-1, keepdims=True)
    spread = jnp.mean(center * center, axis=-1, keepdims=True)
    return center * lax.rsqrt(spread + EPS) * gain


def attend_block(queries, keys, vectors, segment):
    scale = queries.shape[-1] ** (-0.5)
    scores = jnp.einsum("qhe,khe->hqk", queries, keys, preferred_element_type=jnp.float32) * scale
    visible = segment[:, None] == segment[None, :]
    scores = jnp.where(visible[None, :, :], scores, NEG)
    top = jnp.max(scores, axis=-1, keepdims=True)
    weights = jnp.exp(scores - top)
    probs = (weights / jnp.sum(weights, axis=-1, keepdims=True)).astype(jnp.bfloat16)
    context = jnp.einsum("hqk,khe->qhe", probs, vectors, preferred_element_type=jnp.float32)
    return context.astype(jnp.bfloat16)


def split_heads(projected):
    shaped = projected.reshape(3, projected.shape[1], projected.shape[2] // HEAD_DIM, HEAD_DIM)
    return (shaped[0], shaped[1], shaped[2])


def round8(rows):
    return -(-rows // 8) * 8


def pad_rows(block):
    return jnp.pad(block, ((0, round8(block.shape[0]) - block.shape[0]), (0, 0)))


def owner_rows(owners, n_dp, group_rows):
    slots = 2 * group_rows // n_dp
    owner_col = owners[:, 0]
    chosen = (owner_col[:, None] == jnp.arange(n_dp, dtype=jnp.int32)[None, :]).astype(jnp.int32)
    earlier = jnp.cumsum(chosen, axis=0) - chosen
    rank = jnp.sum(earlier * chosen, axis=1)
    target = owner_col * slots + rank
    return (
        jnp.full((n_dp * slots,), group_rows, jnp.int32)
        .at[target]
        .set(jnp.arange(group_rows, dtype=jnp.int32))
    )


def local(tokens, attn_gain, qkv_weight, out_weight, merge_gain, merge_weight, segment_ids, owners):
    tok_rows = tokens.shape[0]
    n_dp = lax.axis_size("dp")
    n_x = lax.axis_size("xx")
    n_in = lax.axis_size("yl") * n_x
    y_low = lax.axis_index("yl")
    lanes = n_in * qkv_weight.shape[-1]
    local_segment = lax.dynamic_slice_in_dim(
        segment_ids, (y_low * n_x + lax.axis_index("xx")) * tok_rows, tok_rows
    )
    slabs = [pad_rows(qkv_weight[c]) for c in range(3)] + [pad_rows(out_weight.T)]
    partner = lax.ppermute(merge_weight, "yl", [(0, 1), (1, 0)])
    stacked = lax.all_gather(jnp.concatenate(slabs, axis=0), ("yl", "xx"), axis=1, tiled=True)
    both = jnp.concatenate([merge_weight, partner], axis=1)
    real = qkv_weight.shape[1]
    tall = round8(real)
    stacked = stacked.reshape(4, tall, lanes)
    merge_rows = -(-both.size // lanes)
    flat = jnp.pad(both.reshape(-1), (0, merge_rows * lanes - both.size))
    flat = flat.reshape(merge_rows, lanes)
    spare = min(4 * (tall - real), merge_rows)
    if spare:
        tail = flat[:spare].reshape(4, spare // 4, lanes)
        tail = jnp.pad(tail, ((0, 0), (0, tall - real - spare // 4), (0, 0)))
        stacked = jnp.concatenate([stacked[:, :real], tail], axis=1)
    rest = flat[spare:]
    extra = -(-rest.shape[0] // tall)
    rest = jnp.pad(rest, ((0, extra * tall - rest.shape[0]), (0, 0))).reshape(extra, tall, lanes)
    payload = jnp.concatenate([stacked, rest], axis=0)
    gathered = lax.all_gather(payload, "dp", axis=0, tiled=False)
    owners, payload = lax.optimization_barrier((owners, payload))
    source_row = owner_rows(owners, n_dp, n_in * tok_rows // 4)
    source_row, tokens = lax.optimization_barrier((source_row, tokens))
    weights = gathered[:, :4]
    merge_full = jnp.concatenate(
        [gathered[:, :4, real:].reshape(n_dp, -1, lanes)[:, :spare], gathered[:, 4:].reshape(n_dp, -1, lanes)],
        axis=1,
    )
    merge_full = merge_full.reshape(n_dp, -1)[:, : both.size].reshape(-1, both.shape[1])
    normed = layer_norm(tokens, attn_gain).astype(jnp.bfloat16)
    normed = normed.reshape(tok_rows, n_dp, -1)
    normed = jnp.pad(normed, ((0, 0), (0, 0), (0, round8(normed.shape[-1]) - normed.shape[-1])))
    projected = jnp.einsum(
        "tgk,gckh->cth",
        normed,
        weights[:, :3],
        preferred_element_type=jnp.float32,
    ).astype(jnp.bfloat16)
    queries, keys, vectors = split_heads(projected)
    context = attend_block(queries, keys, vectors, local_segment).reshape(tok_rows, -1)
    attn_out = jnp.einsum(
        "tf,gkf->tgk", context, weights[:, 3], preferred_element_type=jnp.float32
    )
    attn_out = attn_out[:, :, : tokens.shape[1] // n_dp].reshape(tok_rows, -1)
    hidden = tokens.astype(jnp.float32) + attn_out
    width = 4 * hidden.shape[1]
    quad_sum = jnp.sum(hidden, axis=-1).reshape(-1, 4).sum(axis=-1)
    center = hidden - jnp.repeat(quad_sum / width, 4)[:, None]
    quad_sq = jnp.sum(center * center, axis=-1).reshape(-1, 4).sum(axis=-1)
    scale = jnp.repeat(lax.rsqrt(quad_sq / width + EPS), 4)
    gain = jnp.tile(merge_gain.reshape(4, -1), (tok_rows // 4, 1))
    live = jnp.repeat(local_segment.reshape(-1, 4)[:, 0] >= 0, 4)
    merged = jnp.where(live[:, None], center * scale[:, None] * gain, 0.0).astype(jnp.bfloat16)
    merged = merged.reshape(tok_rows // 4, -1)
    mine = jnp.dot(
        lax.all_gather(merged, "xx", axis=0, tiled=True),
        merge_full,
        preferred_element_type=jnp.float32,
    ).astype(jnp.bfloat16)
    cols = merge_weight.shape[1]
    swapped = lax.ppermute(mine[:, cols:], "yl", [(0, 1), (1, 0)])
    features = jnp.where(
        y_low == 0,
        jnp.concatenate([mine[:, :cols], swapped], axis=0),
        jnp.concatenate([swapped, mine[:, :cols]], axis=0),
    )
    group_rows = features.shape[0]
    pick = (source_row[:, None] == jnp.arange(group_rows, dtype=jnp.int32)[None, :]).astype(jnp.bfloat16)
    outgoing = jnp.dot(pick, features, preferred_element_type=jnp.float32).astype(jnp.bfloat16)
    return lax.all_to_all(outgoing, "dp", split_axis=0, concat_axis=0, tiled=True)


def solution(mesh):
    dp, inner = "dp", ("yl", "xx")
    n_dp, n_in = mesh.shape["dp"], mesh.shape["inner"]
    split = Mesh(mesh.devices.reshape(n_dp, 2, n_in // 2), ("dp", "yl", "xx"))
    placed = (
        P((dp, *inner), None),
        P(),
        P(None, dp, inner),
        P(inner, dp),
        P(),
        P(dp, inner),
        P(dp),
        P(dp, None),
    )
    return jax.shard_map(
        local, mesh=split, in_specs=placed, out_specs=P(dp, inner), check_vma=False
    )
```

```python
import jax
import jax.numpy as jnp
from jax import lax
from jax.sharding import Mesh, PartitionSpec as P

HEAD_DIM = 104


EPS = 1e-06
NEG = -1e30


def layer_norm(values, gain):
    values = values.astype(jnp.float32)
    center = values - jnp.mean(values, axis=-1, keepdims=True)
    spread = jnp.mean(center * center, axis=-1, keepdims=True)
    return center * lax.rsqrt(spread + EPS) * gain


def attend_block(queries, keys, vectors, segment):
    scale = queries.shape[-1] ** (-0.5)
    scores = jnp.einsum("qhe,khe->hqk", queries, keys, preferred_element_type=jnp.float32) * scale
    visible = segment[:, None] == segment[None, :]
    scores = jnp.where(visible[None, :, :], scores, NEG)
    top = jnp.max(scores, axis=-1, keepdims=True)
    weights = jnp.exp(scores - top)
    probs = (weights / jnp.sum(weights, axis=-1, keepdims=True)).astype(jnp.bfloat16)
    context = jnp.einsum("hqk,khe->qhe", probs, vectors, preferred_element_type=jnp.float32)
    return context.astype(jnp.bfloat16)


def split_heads(projected):
    shaped = projected.reshape(3, projected.shape[1], projected.shape[2] // HEAD_DIM, HEAD_DIM)
    return (shaped[0], shaped[1], shaped[2])


def round8(rows):
    return -(-rows // 8) * 8


def pad_rows(block):
    return jnp.pad(block, ((0, round8(block.shape[0]) - block.shape[0]), (0, 0)))


def owner_rows(owners, n_dp, group_rows):
    slots = 2 * group_rows // n_dp
    owner_col = owners[:, 0]
    chosen = (owner_col[:, None] == jnp.arange(n_dp, dtype=jnp.int32)[None, :]).astype(jnp.int32)
    earlier = jnp.cumsum(chosen, axis=0) - chosen
    rank = jnp.sum(earlier * chosen, axis=1)
    target = owner_col * slots + rank
    return (
        jnp.full((n_dp * slots,), group_rows, jnp.int32)
        .at[target]
        .set(jnp.arange(group_rows, dtype=jnp.int32))
    )


def local(tokens, attn_gain, qkv_weight, out_weight, merge_gain, merge_weight, segment_ids, owners):
    tok_rows = tokens.shape[0]
    n_dp = lax.axis_size("dp")
    n_x = lax.axis_size("xx")
    n_in = lax.axis_size("yl") * n_x
    y_low = lax.axis_index("yl")
    lanes = n_in * qkv_weight.shape[-1]
    local_segment = lax.dynamic_slice_in_dim(
        segment_ids, (y_low * n_x + lax.axis_index("xx")) * tok_rows, tok_rows
    )
    slabs = [pad_rows(qkv_weight[c]) for c in range(3)] + [pad_rows(out_weight.T)]
    partner = lax.ppermute(merge_weight, "yl", [(0, 1), (1, 0)])
    stacked = lax.all_gather(jnp.concatenate(slabs, axis=0), ("yl", "xx"), axis=1, tiled=True)
    both = jnp.concatenate([merge_weight, partner], axis=1)
    real = qkv_weight.shape[1]
    tall = round8(real)
    stacked = stacked.reshape(4, tall, lanes)
    merge_rows = -(-both.size // lanes)
    flat = jnp.pad(both.reshape(-1), (0, merge_rows * lanes - both.size))
    flat = flat.reshape(merge_rows, lanes)
    spare = min(4 * (tall - real), merge_rows)
    if spare:
        tail = flat[:spare].reshape(4, spare // 4, lanes)
        tail = jnp.pad(tail, ((0, 0), (0, tall - real - spare // 4), (0, 0)))
        stacked = jnp.concatenate([stacked[:, :real], tail], axis=1)
    rest = flat[spare:]
    extra = -(-rest.shape[0] // tall)
    rest = jnp.pad(rest, ((0, extra * tall - rest.shape[0]), (0, 0))).reshape(extra, tall, lanes)
    payload = jnp.concatenate([stacked, rest], axis=0)
    gathered = lax.all_gather(payload, "dp", axis=0, tiled=False)
    owners, payload = lax.optimization_barrier((owners, payload))
    source_row = owner_rows(owners, n_dp, n_in * tok_rows // 4)
    source_row, tokens = lax.optimization_barrier((source_row, tokens))
    weights = gathered[:, :4]
    merge_full = jnp.concatenate(
        [gathered[:, :4, real:].reshape(n_dp, -1, lanes)[:, :spare], gathered[:, 4:].reshape(n_dp, -1, lanes)],
        axis=1,
    )
    merge_full = merge_full.reshape(n_dp, -1)[:, : both.size].reshape(-1, both.shape[1])
    normed = layer_norm(tokens, attn_gain).astype(jnp.bfloat16)
    normed = normed.reshape(tok_rows, n_dp, -1)
    normed = jnp.pad(normed, ((0, 0), (0, 0), (0, round8(normed.shape[-1]) - normed.shape[-1])))
    projected = jnp.einsum(
        "tgk,gckh->cth",
        normed,
        weights[:, :3],
        preferred_element_type=jnp.float32,
    ).astype(jnp.bfloat16)
    queries, keys, vectors = split_heads(projected)
    context = attend_block(queries, keys, vectors, local_segment).reshape(tok_rows, -1)
    attn_out = jnp.einsum(
        "tf,gkf->tgk", context, weights[:, 3], preferred_element_type=jnp.float32
    )
    attn_out = attn_out[:, :, : tokens.shape[1] // n_dp].reshape(tok_rows, -1)
    hidden = tokens.astype(jnp.float32) + attn_out
    width = 4 * hidden.shape[1]
    quad_sum = jnp.sum(hidden, axis=-1).reshape(-1, 4).sum(axis=-1)
    center = hidden - jnp.repeat(quad_sum / width, 4)[:, None]
    quad_sq = jnp.sum(center * center, axis=-1).reshape(-1, 4).sum(axis=-1)
    scale = jnp.repeat(lax.rsqrt(quad_sq / width + EPS), 4)
    gain = jnp.tile(merge_gain.reshape(4, -1), (tok_rows // 4, 1))
    live = jnp.repeat(local_segment.reshape(-1, 4)[:, 0] >= 0, 4)
    merged = jnp.where(live[:, None], center * scale[:, None] * gain, 0.0).astype(jnp.bfloat16)
    merged = merged.reshape(tok_rows // 4, -1)
    rows_x = lax.all_gather(merged, "xx", axis=0, tiled=True)
    cols = merge_weight.shape[1]
    theirs = jnp.dot(rows_x, merge_full[:, cols:], preferred_element_type=jnp.float32)
    swapped = lax.ppermute(theirs.astype(jnp.bfloat16), "yl", [(0, 1), (1, 0)])
    own = jnp.dot(rows_x, merge_full[:, :cols], preferred_element_type=jnp.float32)
    own, swapped = lax.optimization_barrier((own.astype(jnp.bfloat16), swapped))
    features = jnp.where(
        y_low == 0,
        jnp.concatenate([own, swapped], axis=0),
        jnp.concatenate([swapped, own], axis=0),
    )
    group_rows = features.shape[0]
    pick = (source_row[:, None] == jnp.arange(group_rows, dtype=jnp.int32)[None, :]).astype(jnp.bfloat16)
    outgoing = jnp.dot(pick, features, preferred_element_type=jnp.float32).astype(jnp.bfloat16)
    return lax.all_to_all(outgoing, "dp", split_axis=0, concat_axis=0, tiled=True)


def solution(mesh):
    dp, inner = "dp", ("yl", "xx")
    n_dp, n_in = mesh.shape["dp"], mesh.shape["inner"]
    split = Mesh(mesh.devices.reshape(n_dp, 2, n_in // 2), ("dp", "yl", "xx"))
    placed = (
        P((dp, *inner), None),
        P(),
        P(None, dp, inner),
        P(inner, dp),
        P(),
        P(dp, inner),
        P(dp),
        P(dp, None),
    )
    return jax.shard_map(
        local, mesh=split, in_specs=placed, out_specs=P(dp, inner), check_vma=False
    )
```

```python
import jax
import jax.numpy as jnp
from jax import lax
from jax.sharding import Mesh, PartitionSpec as P

HEAD_DIM = 104


EPS = 1e-06
NEG = -1e30


def layer_norm(values, gain):
    values = values.astype(jnp.float32)
    center = values - jnp.mean(values, axis=-1, keepdims=True)
    spread = jnp.mean(center * center, axis=-1, keepdims=True)
    return center * lax.rsqrt(spread + EPS) * gain


def attend_block(queries, keys, vectors, segment):
    scale = queries.shape[-1] ** (-0.5)
    scores = jnp.einsum("qhe,khe->hqk", queries, keys, preferred_element_type=jnp.float32) * scale
    visible = segment[:, None] == segment[None, :]
    scores = jnp.where(visible[None, :, :], scores, NEG)
    top = jnp.max(scores, axis=-1, keepdims=True)
    weights = jnp.exp(scores - top)
    probs = (weights / jnp.sum(weights, axis=-1, keepdims=True)).astype(jnp.bfloat16)
    context = jnp.einsum("hqk,khe->qhe", probs, vectors, preferred_element_type=jnp.float32)
    return context.astype(jnp.bfloat16)


def split_heads(projected):
    shaped = projected.reshape(3, projected.shape[1], projected.shape[2] // HEAD_DIM, HEAD_DIM)
    return (shaped[0], shaped[1], shaped[2])


def round8(rows):
    return -(-rows // 8) * 8


def pad_rows(block):
    return jnp.pad(block, ((0, round8(block.shape[0]) - block.shape[0]), (0, 0)))


def owner_rows(owners, n_dp, group_rows):
    slots = 2 * group_rows // n_dp
    owner_col = owners[:, 0]
    chosen = (owner_col[:, None] == jnp.arange(n_dp, dtype=jnp.int32)[None, :]).astype(jnp.int32)
    earlier = jnp.cumsum(chosen, axis=0) - chosen
    rank = jnp.sum(earlier * chosen, axis=1)
    target = owner_col * slots + rank
    return (
        jnp.full((n_dp * slots,), group_rows, jnp.int32)
        .at[target]
        .set(jnp.arange(group_rows, dtype=jnp.int32))
    )


def local(tokens, attn_gain, qkv_weight, out_weight, merge_gain, merge_weight, segment_ids, owners):
    tok_rows = tokens.shape[0]
    n_dp = lax.axis_size("dp")
    n_x = lax.axis_size("xx")
    n_in = lax.axis_size("yl") * n_x
    y_low = lax.axis_index("yl")
    lanes = n_in * qkv_weight.shape[-1]
    local_segment = lax.dynamic_slice_in_dim(
        segment_ids, (y_low * n_x + lax.axis_index("xx")) * tok_rows, tok_rows
    )
    slabs = [pad_rows(qkv_weight[c]) for c in range(3)] + [pad_rows(out_weight.T)]
    stacked = lax.all_gather(jnp.concatenate(slabs, axis=0), ("yl", "xx"), axis=1, tiled=True)
    both = merge_weight
    real = qkv_weight.shape[1]
    tall = round8(real)
    stacked = stacked.reshape(4, tall, lanes)
    merge_rows = -(-both.size // lanes)
    flat = jnp.pad(both.reshape(-1), (0, merge_rows * lanes - both.size))
    flat = flat.reshape(merge_rows, lanes)
    spare = min(4 * (tall - real), merge_rows // 4 * 4)
    if spare:
        tail = flat[:spare].reshape(4, spare // 4, lanes)
        tail = jnp.pad(tail, ((0, 0), (0, tall - real - spare // 4), (0, 0)))
        stacked = jnp.concatenate([stacked[:, :real], tail], axis=1)
    rest = flat[spare:]
    extra = -(-rest.shape[0] // tall)
    rest = jnp.pad(rest, ((0, extra * tall - rest.shape[0]), (0, 0))).reshape(extra, tall, lanes)
    payload = jnp.concatenate([stacked, rest], axis=0)
    gathered = lax.all_gather(payload, "dp", axis=0, tiled=False)
    owners, payload = lax.optimization_barrier((owners, payload))
    source_row = owner_rows(owners, n_dp, n_in * tok_rows // 4)
    source_row, tokens = lax.optimization_barrier((source_row, tokens))
    weights = gathered[:, :4]
    merge_full = jnp.concatenate(
        [
            gathered[:, :4, real : real + spare // 4].reshape(n_dp, -1, lanes),
            gathered[:, 4:].reshape(n_dp, -1, lanes),
        ],
        axis=1,
    )
    merge_full = merge_full.reshape(n_dp, -1)[:, : both.size].reshape(-1, both.shape[1])
    normed = layer_norm(tokens, attn_gain).astype(jnp.bfloat16)
    normed = normed.reshape(tok_rows, n_dp, -1)
    normed = jnp.pad(normed, ((0, 0), (0, 0), (0, round8(normed.shape[-1]) - normed.shape[-1])))
    projected = jnp.einsum(
        "tgk,gckh->cth",
        normed,
        weights[:, :3],
        preferred_element_type=jnp.float32,
    ).astype(jnp.bfloat16)
    queries, keys, vectors = split_heads(projected)
    context = attend_block(queries, keys, vectors, local_segment).reshape(tok_rows, -1)
    attn_out = jnp.einsum(
        "tf,gkf->tgk", context, weights[:, 3], preferred_element_type=jnp.float32
    )
    attn_out = attn_out[:, :, : tokens.shape[1] // n_dp].reshape(tok_rows, -1)
    hidden = tokens.astype(jnp.float32) + attn_out
    width = 4 * hidden.shape[1]
    quad_sum = jnp.sum(hidden, axis=-1).reshape(-1, 4).sum(axis=-1)
    center = hidden - jnp.repeat(quad_sum / width, 4)[:, None]
    quad_sq = jnp.sum(center * center, axis=-1).reshape(-1, 4).sum(axis=-1)
    scale = jnp.repeat(lax.rsqrt(quad_sq / width + EPS), 4)
    gain = jnp.tile(merge_gain.reshape(4, -1), (tok_rows // 4, 1))
    live = jnp.repeat(local_segment.reshape(-1, 4)[:, 0] >= 0, 4)
    merged = jnp.where(live[:, None], center * scale[:, None] * gain, 0.0).astype(jnp.bfloat16)
    merged = merged.reshape(tok_rows // 4, -1)
    rows_x = lax.all_gather(merged, "xx", axis=0, tiled=True)
    cols = merge_weight.shape[1]
    partner = lax.ppermute(merge_full, "yl", [(0, 1), (1, 0)])
    theirs = jnp.dot(rows_x, partner, preferred_element_type=jnp.float32)
    swapped = lax.ppermute(theirs.astype(jnp.bfloat16), "yl", [(0, 1), (1, 0)])
    own = jnp.dot(rows_x, merge_full, preferred_element_type=jnp.float32)
    own, swapped = lax.optimization_barrier((own.astype(jnp.bfloat16), swapped))
    features = jnp.where(
        y_low == 0,
        jnp.concatenate([own, swapped], axis=0),
        jnp.concatenate([swapped, own], axis=0),
    )
    group_rows = features.shape[0]
    pick = (source_row[:, None] == jnp.arange(group_rows, dtype=jnp.int32)[None, :]).astype(jnp.bfloat16)
    outgoing = jnp.dot(pick, features, preferred_element_type=jnp.float32).astype(jnp.bfloat16)
    return lax.all_to_all(outgoing, "dp", split_axis=0, concat_axis=0, tiled=True)


def solution(mesh):
    dp, inner = "dp", ("yl", "xx")
    n_dp, n_in = mesh.shape["dp"], mesh.shape["inner"]
    split = Mesh(mesh.devices.reshape(n_dp, 2, n_in // 2), ("dp", "yl", "xx"))
    placed = (
        P((dp, *inner), None),
        P(),
        P(None, dp, inner),
        P(inner, dp),
        P(),
        P(dp, inner),
        P(dp),
        P(dp, None),
    )
    return jax.shard_map(
        local, mesh=split, in_specs=placed, out_specs=P(dp, inner), check_vma=False
    )
```

```python
import jax
import jax.numpy as jnp
from jax import lax
from jax.sharding import Mesh, PartitionSpec as P

HEAD_DIM = 104


EPS = 1e-06
NEG = -1e30


def layer_norm(values, gain):
    values = values.astype(jnp.float32)
    center = values - jnp.mean(values, axis=-1, keepdims=True)
    spread = jnp.mean(center * center, axis=-1, keepdims=True)
    return center * lax.rsqrt(spread + EPS) * gain


def attend_block(queries, keys, vectors, segment):
    scale = queries.shape[-1] ** (-0.5)
    scores = jnp.einsum("qhe,khe->hqk", queries, keys, preferred_element_type=jnp.float32) * scale
    visible = segment[:, None] == segment[None, :]
    scores = jnp.where(visible[None, :, :], scores, NEG)
    top = jnp.max(scores, axis=-1, keepdims=True)
    weights = jnp.exp(scores - top)
    probs = (weights / jnp.sum(weights, axis=-1, keepdims=True)).astype(jnp.bfloat16)
    context = jnp.einsum("hqk,khe->qhe", probs, vectors, preferred_element_type=jnp.float32)
    return context.astype(jnp.bfloat16)


def split_heads(projected):
    shaped = projected.reshape(3, projected.shape[1], projected.shape[2] // HEAD_DIM, HEAD_DIM)
    return (shaped[0], shaped[1], shaped[2])


def round8(rows):
    return -(-rows // 8) * 8


def pad_rows(block):
    return jnp.pad(block, ((0, round8(block.shape[0]) - block.shape[0]), (0, 0)))


def owner_rows(owners, n_dp, group_rows):
    slots = 2 * group_rows // n_dp
    owner_col = owners[:, 0]
    chosen = (owner_col[:, None] == jnp.arange(n_dp, dtype=jnp.int32)[None, :]).astype(jnp.int32)
    earlier = jnp.cumsum(chosen, axis=0) - chosen
    rank = jnp.sum(earlier * chosen, axis=1)
    target = owner_col * slots + rank
    return (
        jnp.full((n_dp * slots,), group_rows, jnp.int32)
        .at[target]
        .set(jnp.arange(group_rows, dtype=jnp.int32))
    )


def local(tokens, attn_gain, qkv_weight, out_weight, merge_gain, merge_weight, segment_ids, owners):
    tok_rows = tokens.shape[0]
    n_dp = lax.axis_size("dp")
    n_x = lax.axis_size("xx")
    n_in = lax.axis_size("yl") * n_x
    y_low = lax.axis_index("yl")
    lanes = n_in * qkv_weight.shape[-1]
    local_segment = lax.dynamic_slice_in_dim(
        segment_ids, (y_low * n_x + lax.axis_index("xx")) * tok_rows, tok_rows
    )
    slabs = [pad_rows(qkv_weight[c]) for c in range(3)] + [pad_rows(out_weight.T)]
    partner = lax.ppermute(merge_weight, "yl", [(0, 1), (1, 0)])
    stacked = lax.all_gather(jnp.concatenate(slabs, axis=0), ("yl", "xx"), axis=1, tiled=True)
    both = jnp.concatenate([merge_weight, partner], axis=1)
    real = qkv_weight.shape[1]
    tall = round8(real)
    stacked = stacked.reshape(4, tall, lanes)
    merge_rows = -(-both.size // lanes)
    flat = jnp.pad(both.reshape(-1), (0, merge_rows * lanes - both.size))
    flat = flat.reshape(merge_rows, lanes)
    spare = min(4 * (tall - real), merge_rows)
    if spare:
        tail = flat[:spare].reshape(4, spare // 4, lanes)
        tail = jnp.pad(tail, ((0, 0), (0, tall - real - spare // 4), (0, 0)))
        stacked = jnp.concatenate([stacked[:, :real], tail], axis=1)
    rest = flat[spare:]
    extra = -(-rest.shape[0] // tall)
    rest = jnp.pad(rest, ((0, extra * tall - rest.shape[0]), (0, 0))).reshape(extra, tall, lanes)
    payload = jnp.concatenate([stacked, rest], axis=0)
    gathered = lax.all_gather(payload, "dp", axis=0, tiled=False)
    owners, payload = lax.optimization_barrier((owners, payload))
    source_row = owner_rows(owners, n_dp, n_in * tok_rows // 4)
    source_row, tokens = lax.optimization_barrier((source_row, tokens))
    weights = gathered[:, :4]
    merge_full = jnp.concatenate(
        [gathered[:, :4, real:].reshape(n_dp, -1, lanes)[:, :spare], gathered[:, 4:].reshape(n_dp, -1, lanes)],
        axis=1,
    )
    merge_full = merge_full.reshape(n_dp, -1)[:, : both.size].reshape(-1, both.shape[1])
    normed = layer_norm(tokens, attn_gain).astype(jnp.bfloat16)
    normed = normed.reshape(tok_rows, n_dp, -1)
    normed = jnp.pad(normed, ((0, 0), (0, 0), (0, round8(normed.shape[-1]) - normed.shape[-1])))
    projected = jnp.einsum(
        "tgk,gckh->cth",
        normed,
        weights[:, :3],
        preferred_element_type=jnp.float32,
    ).astype(jnp.bfloat16)
    queries, keys, vectors = split_heads(projected)
    context = attend_block(queries, keys, vectors, local_segment).reshape(tok_rows, -1)
    attn_out = jnp.einsum(
        "tf,gkf->tgk", context, weights[:, 3], preferred_element_type=jnp.float32
    )
    attn_out = attn_out[:, :, : tokens.shape[1] // n_dp].reshape(tok_rows, -1)
    hidden = tokens.astype(jnp.float32) + attn_out
    width = 4 * hidden.shape[1]
    quad_sum = jnp.sum(hidden, axis=-1).reshape(-1, 4).sum(axis=-1)
    center = hidden - jnp.repeat(quad_sum / width, 4)[:, None]
    quad_sq = jnp.sum(center * center, axis=-1).reshape(-1, 4).sum(axis=-1)
    scale = jnp.repeat(lax.rsqrt(quad_sq / width + EPS), 4)
    gain = jnp.tile(merge_gain.reshape(4, -1), (tok_rows // 4, 1))
    live = jnp.repeat(local_segment.reshape(-1, 4)[:, 0] >= 0, 4)
    merged = jnp.where(live[:, None], center * scale[:, None] * gain, 0.0).astype(jnp.bfloat16)
    merged = merged.reshape(tok_rows // 4, -1)
    rows_x = lax.all_gather(merged, "xx", axis=0, tiled=True)
    cols = merge_weight.shape[1]
    theirs = jnp.dot(rows_x, merge_full[:, cols:], preferred_element_type=jnp.float32)
    swapped = lax.ppermute(theirs.astype(jnp.bfloat16), "yl", [(0, 1), (1, 0)])
    own = jnp.dot(rows_x, merge_full[:, :cols], preferred_element_type=jnp.float32)
    own = own.astype(jnp.bfloat16)
    half = own.shape[0]
    group_rows = 2 * half
    pick = (source_row[:, None] == jnp.arange(group_rows, dtype=jnp.int32)[None, :]).astype(jnp.bfloat16)
    first = y_low == 0
    pick_own = jnp.where(first, pick[:, :half], pick[:, half:])
    pick_swap = jnp.where(first, pick[:, half:], pick[:, :half])
    part = jnp.dot(pick_own, own, preferred_element_type=jnp.float32)
    outgoing = part + jnp.dot(pick_swap, swapped, preferred_element_type=jnp.float32)
    outgoing = outgoing.astype(jnp.bfloat16)
    return lax.all_to_all(outgoing, "dp", split_axis=0, concat_axis=0, tiled=True)


def solution(mesh):
    dp, inner = "dp", ("yl", "xx")
    n_dp, n_in = mesh.shape["dp"], mesh.shape["inner"]
    split = Mesh(mesh.devices.reshape(n_dp, 2, n_in // 2), ("dp", "yl", "xx"))
    placed = (
        P((dp, *inner), None),
        P(),
        P(None, dp, inner),
        P(inner, dp),
        P(),
        P(dp, inner),
        P(dp),
        P(dp, None),
    )
    return jax.shard_map(
        local, mesh=split, in_specs=placed, out_specs=P(dp, inner), check_vma=False
    )
```
